1024 devices in a mesh: gx: 4 (over x), gy: 8 (over y, core), gz: 32 (over z).
Axes of the slice: x: 4, y: 4, z: 32, core: 2. Of those that a mesh axis runs over, the one named last changes fastest.
Arguments:
- right_side: float32 [32, 128, 8192], P('gx', 'gy', 'gz'), may hold values from -6 to 6
- coefficient: float32 [32, 128, 8192], P('gx', 'gy', 'gz'), may hold values from 0.3 to 3
- agg_weight: float32 [32, 128, 8192], P('gx', 'gy', 'gz'), may hold values from 0.03 to 0.1
- coarse_factor: float32 [8192, 8192], P(('gx', 'gy', 'gz')), may hold values from -0.25 to 0.25
Outputs:
- pressure_update: float32 [32, 128, 8192], P('gx', 'gy', 'gz')
- coarse_solution: float32 [8192], P(('gx', 'gy', 'gz'))
The draws below stay inside these ranges and needn't reach their ends.
All inputs are finite; a program needn't handle non-finite values.
Results may differ from the reference program's by a relative error of at most 0.00024.
Values sent between devices are 32-bit elements; how exact they have to be, the bound alone decides.
No kernel may reach another device: no remote copies, remote signals or barrier semaphores. Data moves between devices by JAX's collectives and lax.ppermute only.
A program may use at most 32 MiB of HBM per device.

```python
import math
import jax
import jax.numpy as jnp
import numpy as np
from jax import lax

ORDER = 7
CHEB = 4
CPD = 8
EXP = 8
EYP = 16
NX = 32
NY = 128
NZ = 8192
AGG = 32
NC = 8192
N_GX = 4
N_GY = 8
N_GZ = 32


def raised(drawn, key, source, target, blocks, factor):
    owner, partner = [(jnp.arange(drawn.shape[dim]) // (drawn.shape[dim] // blocks)).reshape([-1 if axis == dim else 1 for axis in range(drawn.ndim)]) for dim in (source, target)]
    chosen = jax.random.permutation(key, blocks)[partner]
    strong = (owner == chosen) | (owner == (partner + blocks // 2) % blocks)
    return jnp.where(strong, factor * drawn, drawn)


def steps_of(rng, dims, cuts, low, top_value):
    def one(dim, blocks):
        draws = jax.random.uniform(jax.random.fold_in(jax.random.fold_in(rng, 6), dim), (blocks,), jnp.float32, low / len(cuts), top_value / len(cuts))
        return jnp.repeat(jnp.exp(draws), dims[dim] // blocks).reshape((-1,) + (1,) * (len(dims) - dim - 1))

    gain = one(*cuts[0])
    for cut in cuts[1:]:
        gain = gain * one(*cut)
    return gain


def scatter_about(rng, dims, scale, bound, split=(), held_as=jnp.bfloat16):
    drawn = jax.random.normal(rng, dims, jnp.float32) * scale
    if len(split) > 0:
        drawn = steps_of(rng, dims, split, -0.22, 0.18) * drawn
    return jnp.clip(drawn, min=-bound, max=bound).astype(held_as)


def heavy_noise(rng, shape, scale, reach, shards, heavy, held_as=jnp.bfloat16):
    values = scale * jax.random.normal(rng, shape, jnp.float32)
    if shards:
        values = values * steps_of(rng, shape, shards, -0.22, 0.18)
    return jnp.clip(raised(values, jax.random.fold_in(rng, 3), *heavy), -reach, reach).astype(held_as)


def setup_inputs(seed: int = 0) -> dict:
    arg_keys = jax.random.split(jax.random.key(seed), 5)
    right_side = scatter_about(arg_keys[0], (NX, NY, NZ), 1.0, 6.0, ((0, 4), (1, 8), (2, 32)), jnp.float32)
    coefficient = jnp.clip(jnp.exp(math.log(3.0) - 2.3025851 * jax.random.uniform(arg_keys[1], (NX, NY, NZ), jnp.float32) ** steps_of(arg_keys[1], (NX, NY, NZ), ((0, 4), (1, 8), (2, 32)), -0.2, 0.2)), 0.3, 3.0)
    agg_weight = jnp.clip(0.03 + 0.07 * jax.random.uniform(arg_keys[2], (NX, NY, NZ), jnp.float32) ** steps_of(arg_keys[2], (NX, NY, NZ), ((0, 4), (1, 8), (2, 32)), -0.2, 0.2), 0.03, 0.1)
    coarse_factor = heavy_noise(arg_keys[3], (NC, NC), NC ** -0.5, 0.25, ((0, 1024),), (0, 1, 1024, 6.0), jnp.float32)
    return dict(right_side=right_side, coefficient=coefficient, agg_weight=agg_weight, coarse_factor=coarse_factor)


highest = lax.Precision.HIGHEST
eig_high = 4.0
eig_low = 0.2
gll_inner = np.array([-0.8717401485096066153, -0.5917001814331423022, -0.2092992179024788687, 0.2092992179024788687, 0.5917001814331423022, 0.8717401485096066153])


def legendre_value(nodes, degree):
    previous = nodes * 0.0 + 1.0
    current = nodes
    for step in range(1, degree):
        following = ((2.0 * step + 1.0) * nodes * current - step * previous) / (step + 1.0)
        previous = current
        current = following
    return current


def gll_tables(poly_order):
    point_count = poly_order + 1
    gll_nodes = np.concatenate([np.array([-1.0]), gll_inner, np.array([1.0])])
    at_nodes = legendre_value(gll_nodes, poly_order)
    weights = 2.0 / (poly_order * point_count * at_nodes ** 2)
    differences = gll_nodes[:, None] - gll_nodes[None, :] + np.eye(point_count)
    derivative = at_nodes[:, None] / (at_nodes[None, :] * differences) * (1.0 - np.eye(point_count))
    end_value = poly_order * point_count / 4.0
    end_row = np.concatenate([np.array([-end_value]), np.zeros(poly_order - 1), np.array([end_value])])
    derivative = derivative + np.eye(point_count) * end_row[None, :]
    return derivative, weights


def forward_parts(field, matrix, points):
    size_x, size_y, size_z = field.shape
    grad_x = jnp.einsum("ia,eajk->eijk", matrix, field.reshape(size_x // points, points, size_y, size_z), precision=highest).reshape(field.shape)
    grad_y = jnp.einsum("ja,ieak->iejk", matrix, field.reshape(size_x, size_y // points, points, size_z), precision=highest).reshape(field.shape)
    grad_z = jnp.einsum("ka,ijea->ijek", matrix, field.reshape(size_x, size_y, size_z // points, points), precision=highest).reshape(field.shape)
    return grad_x, grad_y, grad_z


def backward_sum(parts, matrix, points):
    part_x, part_y, part_z = parts
    size_x, size_y, size_z = part_x.shape
    total = jnp.einsum("ai,eajk->eijk", matrix, part_x.reshape(size_x // points, points, size_y, size_z), precision=highest).reshape(part_x.shape)
    total = total + jnp.einsum("aj,ieak->iejk", matrix, part_y.reshape(size_x, size_y // points, points, size_z), precision=highest).reshape(part_x.shape)
    total = total + jnp.einsum("ak,ijea->ijek", matrix, part_z.reshape(size_x, size_y, size_z // points, points), precision=highest).reshape(part_x.shape)
    return total


def combine(padded, axis_dim, length, points):
    own = lax.slice_in_dim(padded, 1, length + 1, axis=axis_dim)
    left = lax.slice_in_dim(padded, 0, length, axis=axis_dim)
    right = lax.slice_in_dim(padded, 2, length + 2, axis=axis_dim)
    shape_list = [1, 1, 1]
    shape_list[axis_dim] = length
    position = (jnp.arange(length, dtype=jnp.int32) % points).reshape(shape_list)
    low_mask = (position == 0).astype(jnp.float32)
    high_mask = (position == points - 1).astype(jnp.float32)
    return own + low_mask * left + high_mask * right


def assemble(field, points):
    size_x, size_y, size_z = field.shape
    padded = jnp.pad(field, 1)
    summed = combine(padded, 0, size_x, points)
    summed = combine(summed, 1, size_y, points)
    return combine(summed, 2, size_z, points)


def reference(right_side, coefficient, agg_weight, coarse_factor):
    points = ORDER + 1
    derivative, weights = gll_tables(ORDER)
    matrix = jnp.asarray(derivative).astype(jnp.float32)
    squared = matrix * matrix
    size_x, size_y, size_z = right_side.shape
    weight_x = jnp.asarray(np.tile(weights, size_x // points)).astype(jnp.float32)
    weight_y = jnp.asarray(np.tile(weights, size_y // points)).astype(jnp.float32)
    weight_z = jnp.asarray(np.tile(weights, size_z // points)).astype(jnp.float32)
    scaled = coefficient * weight_x[:, None, None] * weight_y[None, :, None] * weight_z[None, None, :]
    diagonal = assemble(backward_sum((scaled, scaled, scaled), squared, points), points)
    inverse = 1.0 / diagonal
    theta = (eig_high + eig_low) / 2.0
    delta = (eig_high - eig_low) / 2.0
    sigma = theta / delta
    residual = right_side
    direction = inverse * residual / theta
    smoothed = direction
    rho = 1.0 / sigma
    for sweep in range(CHEB):
        grads = forward_parts(direction, matrix, points)
        local = backward_sum((scaled * grads[0], scaled * grads[1], scaled * grads[2]), matrix, points)
        residual = residual - assemble(local, points)
        if sweep + 1 < CHEB:
            rho_new = 1.0 / (2.0 * sigma - rho)
            direction = rho_new * rho * direction + (2.0 * rho_new / delta) * inverse * residual
            smoothed = smoothed + direction
            rho = rho_new
    weighted = (agg_weight * residual).reshape(N_GX, EXP, N_GY, EYP, N_GZ, CPD, AGG)
    coarse_rhs = jnp.sum(weighted, axis=(1, 3, 6)).reshape(NC)
    projected = jnp.dot(coarse_rhs, coarse_factor, precision=highest)
    coarse_solution = jnp.dot(coarse_factor, projected, precision=highest)
    spread = jnp.broadcast_to(coarse_solution.reshape(N_GX, 1, N_GY, 1, N_GZ, CPD, 1), (N_GX, EXP, N_GY, EYP, N_GZ, CPD, AGG)).reshape(NX, NY, NZ)
    pressure_update = smoothed + agg_weight * spread
    return pressure_update, coarse_solution
```

```python
import jax
import jax.numpy as jnp
import numpy as np
from jax import lax
from jax.sharding import PartitionSpec as P

ORDER = 7
CHEB = 4


highest = lax.Precision.HIGHEST
eig_high = 4.0
eig_low = 0.2
gll_inner = np.array(
    [
        -0.8717401485096066,
        -0.5917001814331423,
        -0.20929921790247888,
        0.20929921790247888,
        0.5917001814331423,
        0.8717401485096066,
    ]
)


def padded_2(cells, sides, width):
    for axis, dim in sides:
        count = lax.axis_size(axis)
        ends = count - 1
        head = lax.slice_in_dim(cells, 0, width, axis=dim)
        tail = lax.slice_in_dim(cells, cells.shape[dim] - width, cells.shape[dim], axis=dim)
        cells = jnp.concatenate(
            [
                lax.ppermute(tail, axis, [(i, (i + 1) % count) for i in range(ends)]),
                cells,
                lax.ppermute(head, axis, [((i + 1) % count, i) for i in range(ends)]),
            ],
            axis=dim,
        )
    return cells


def butterfly_sum(value, axes):
    for axis in axes:
        count = lax.axis_size(axis)
        stride = 1
        while stride < count:
            value = value + lax.ppermute(value, axis, [(i, i ^ stride) for i in range(count)])
            stride *= 2
    return value


def legendre_value(nodes, degree):
    previous = nodes * 0.0 + 1.0
    current = nodes
    for step in range(1, degree):
        following = ((2.0 * step + 1.0) * nodes * current - step * previous) / (step + 1.0)
        previous = current
        current = following
    return current


def gll_tables(poly_order):
    point_count = poly_order + 1
    gll_nodes = np.concatenate([np.array([-1.0]), gll_inner, np.array([1.0])])
    at_nodes = legendre_value(gll_nodes, poly_order)
    weights = 2.0 / (poly_order * point_count * at_nodes**2)
    differences = gll_nodes[:, None] - gll_nodes[None, :] + np.eye(point_count)
    derivative = at_nodes[:, None] / (at_nodes[None, :] * differences) * (1.0 - np.eye(point_count))
    end_value = poly_order * point_count / 4.0
    end_row = np.concatenate(
        [np.array([-end_value]), np.zeros(poly_order - 1), np.array([end_value])]
    )
    derivative = derivative + np.eye(point_count) * end_row[None, :]
    return (derivative, weights)


def forward_parts(field, mats):
    mat_x, mat_y, mat_z = mats
    size_x, size_y, size_z = field.shape
    grad_x = jnp.einsum("ia,ajk->ijk", mat_x, field, precision=highest)
    grad_y = jnp.einsum("ja,iak->ijk", mat_y, field, precision=highest)
    blocks = field.reshape(size_x, size_y, size_z // 128, 128)
    grad_z = jnp.einsum("ca,ijsa->ijsc", mat_z, blocks, precision=highest).reshape(field.shape)
    return (grad_x, grad_y, grad_z)


def backward_sum(parts, mats):
    mat_x, mat_y, mat_z = mats
    part_x, part_y, part_z = parts
    size_x, size_y, size_z = part_x.shape
    total = jnp.einsum("ai,ajk->ijk", mat_x, part_x, precision=highest)
    total = total + jnp.einsum("aj,iak->ijk", mat_y, part_y, precision=highest)
    blocks = part_z.reshape(size_x, size_y, size_z // 128, 128)
    total = total + jnp.einsum("ac,ijsa->ijsc", mat_z, blocks, precision=highest).reshape(
        part_x.shape
    )
    return total


def combine(padded, axis_dim, length, points):
    own = lax.slice_in_dim(padded, 1, length + 1, axis=axis_dim)
    left = lax.slice_in_dim(padded, 0, length, axis=axis_dim)
    right = lax.slice_in_dim(padded, 2, length + 2, axis=axis_dim)
    shape_list = [1, 1, 1]
    shape_list[axis_dim] = length
    position = (jnp.arange(length, dtype=jnp.int32) % points).reshape(shape_list)
    low_mask = (position == 0).astype(jnp.float32)
    high_mask = (position == points - 1).astype(jnp.float32)
    return own + low_mask * left + high_mask * right


def assemble(field, points):
    size_x, size_y, size_z = field.shape
    padded = padded_2(field, (("gx", 0), ("gy", 1), ("gz", 2)), 1)
    summed = combine(padded, 0, size_x, points)
    summed = combine(summed, 1, size_y, points)
    summed = combine(summed, 2, size_z, points)
    return summed


def per_device(right_side, coefficient, agg_weight, coarse_factor):
    points = ORDER + 1
    derivative, weights = gll_tables(ORDER)
    size_x, size_y, size_z = right_side.shape
    mat_x = jnp.asarray(np.kron(np.eye(size_x // points), derivative), dtype=jnp.float32)
    mat_y = jnp.asarray(np.kron(np.eye(size_y // points), derivative), dtype=jnp.float32)
    mat_z = jnp.asarray(np.kron(np.eye(128 // points), derivative), dtype=jnp.float32)
    mats = (mat_x, mat_y, mat_z)
    squares = (mat_x * mat_x, mat_y * mat_y, mat_z * mat_z)
    weight_x = jnp.asarray(np.tile(weights, size_x // points), dtype=jnp.float32)
    weight_y = jnp.asarray(np.tile(weights, size_y // points), dtype=jnp.float32)
    weight_z = jnp.asarray(np.tile(weights, size_z // points), dtype=jnp.float32)
    scaled = (
        coefficient * weight_x[:, None, None] * weight_y[None, :, None] * weight_z[None, None, :]
    )
    diagonal = assemble(backward_sum((scaled, scaled, scaled), squares), points)
    inverse = 1.0 / diagonal
    theta = (eig_high + eig_low) / 2.0
    delta = (eig_high - eig_low) / 2.0
    sigma = theta / delta
    residual = right_side
    direction = inverse * residual / theta
    smoothed = direction
    rho = 1.0 / sigma
    for sweep in range(CHEB):
        grads = forward_parts(direction, mats)
        local = backward_sum((scaled * grads[0], scaled * grads[1], scaled * grads[2]), mats)
        residual = residual - assemble(local, points)
        if sweep + 1 < CHEB:
            rho_new = 1.0 / (2.0 * sigma - rho)
            direction = rho_new * rho * direction + 2.0 * rho_new / delta * inverse * residual
            smoothed = smoothed + direction
            rho = rho_new
    aggregates = coarse_factor.shape[0]
    column_sums = jnp.sum(agg_weight * residual, axis=(0, 1))
    coarse_rhs = jnp.sum(column_sums.reshape(aggregates, size_z // aggregates), axis=1)
    partial_term = jnp.dot(coarse_rhs, coarse_factor, precision=highest)
    projected = butterfly_sum(partial_term, ("gy", "gz", "gx"))
    coarse_solution = jnp.dot(coarse_factor, projected, precision=highest)
    spread = jnp.repeat(coarse_solution, size_z // aggregates)
    pressure_update = smoothed + agg_weight * spread[None, None, :]
    return (pressure_update, coarse_solution)


def solution(mesh):
    return jax.shard_map(
        per_device,
        mesh=mesh,
        in_specs=(
            P("gx", "gy", "gz"),
            P("gx", "gy", "gz"),
            P("gx", "gy", "gz"),
            P(("gx", "gy", "gz"), None),
        ),
        out_specs=(P("gx", "gy", "gz"), P(("gx", "gy", "gz"))),
        check_vma=False,
    )
```

```python
import jax
import jax.numpy as jnp
import numpy as np
from jax import lax
from jax.sharding import PartitionSpec as P

ORDER = 7
CHEB = 4


highest = lax.Precision.HIGHEST
eig_high = 4.0
eig_low = 0.2
gll_inner = np.array(
    [
        -0.8717401485096066,
        -0.5917001814331423,
        -0.20929921790247888,
        0.20929921790247888,
        0.5917001814331423,
        0.8717401485096066,
    ]
)


def padded_2(cells, sides, width):
    for axis, dim in sides:
        count = lax.axis_size(axis)
        ends = count - 1
        head = lax.slice_in_dim(cells, 0, width, axis=dim)
        tail = lax.slice_in_dim(cells, cells.shape[dim] - width, cells.shape[dim], axis=dim)
        from_prev = lax.ppermute(jnp.squeeze(tail, dim), axis, [(i, i + 1) for i in range(ends)])
        from_next = lax.ppermute(jnp.squeeze(head, dim), axis, [(i + 1, i) for i in range(ends)])
        cells = jnp.concatenate(
            [jnp.expand_dims(from_prev, dim), cells, jnp.expand_dims(from_next, dim)],
            axis=dim,
        )
    return cells


def butterfly_sum(value, axes):
    for axis in axes:
        count = lax.axis_size(axis)
        stride = 1
        while stride < count:
            value = value + lax.ppermute(value, axis, [(i, i ^ stride) for i in range(count)])
            stride *= 2
    return value


def legendre_value(nodes, degree):
    previous = nodes * 0.0 + 1.0
    current = nodes
    for step in range(1, degree):
        following = ((2.0 * step + 1.0) * nodes * current - step * previous) / (step + 1.0)
        previous = current
        current = following
    return current


def gll_tables(poly_order):
    point_count = poly_order + 1
    gll_nodes = np.concatenate([np.array([-1.0]), gll_inner, np.array([1.0])])
    at_nodes = legendre_value(gll_nodes, poly_order)
    weights = 2.0 / (poly_order * point_count * at_nodes**2)
    differences = gll_nodes[:, None] - gll_nodes[None, :] + np.eye(point_count)
    derivative = at_nodes[:, None] / (at_nodes[None, :] * differences) * (1.0 - np.eye(point_count))
    end_value = poly_order * point_count / 4.0
    end_row = np.concatenate(
        [np.array([-end_value]), np.zeros(poly_order - 1), np.array([end_value])]
    )
    derivative = derivative + np.eye(point_count) * end_row[None, :]
    return (derivative, weights)


def forward_parts(field, mats):
    mat_x, mat_y, mat_z = mats
    size_x, size_y, size_z = field.shape
    grad_x = jnp.einsum("ia,ajk->ijk", mat_x, field, precision=highest)
    grad_y = jnp.einsum("ja,iak->ijk", mat_y, field, precision=highest)
    blocks = field.reshape(size_x, size_y, size_z // 128, 128)
    grad_z = jnp.einsum("ca,ijsa->ijsc", mat_z, blocks, precision=highest).reshape(field.shape)
    return (grad_x, grad_y, grad_z)


def backward_sum(parts, mats):
    mat_x, mat_y, mat_z = mats
    part_x, part_y, part_z = parts
    size_x, size_y, size_z = part_x.shape
    total = jnp.einsum("ai,ajk->ijk", mat_x, part_x, precision=highest)
    total = total + jnp.einsum("aj,iak->ijk", mat_y, part_y, precision=highest)
    blocks = part_z.reshape(size_x, size_y, size_z // 128, 128)
    total = total + jnp.einsum("ac,ijsa->ijsc", mat_z, blocks, precision=highest).reshape(
        part_x.shape
    )
    return total


def combine(padded, axis_dim, length, points):
    own = lax.slice_in_dim(padded, 1, length + 1, axis=axis_dim)
    left = lax.slice_in_dim(padded, 0, length, axis=axis_dim)
    right = lax.slice_in_dim(padded, 2, length + 2, axis=axis_dim)
    shape_list = [1, 1, 1]
    shape_list[axis_dim] = length
    position = (jnp.arange(length, dtype=jnp.int32) % points).reshape(shape_list)
    low_mask = (position == 0).astype(jnp.float32)
    high_mask = (position == points - 1).astype(jnp.float32)
    return own + low_mask * left + high_mask * right


def assemble(field, points):
    size_x, size_y, size_z = field.shape
    padded = padded_2(field, (("gz", 2), ("gy", 1), ("gx", 0)), 1)
    summed = combine(padded, 0, size_x, points)
    summed = combine(summed, 1, size_y, points)
    summed = combine(summed, 2, size_z, points)
    return summed


def per_device(right_side, coefficient, agg_weight, coarse_factor):
    points = ORDER + 1
    derivative, weights = gll_tables(ORDER)
    size_x, size_y, size_z = right_side.shape
    mat_x = jnp.asarray(np.kron(np.eye(size_x // points), derivative), dtype=jnp.float32)
    mat_y = jnp.asarray(np.kron(np.eye(size_y // points), derivative), dtype=jnp.float32)
    mat_z = jnp.asarray(np.kron(np.eye(128 // points), derivative), dtype=jnp.float32)
    mats = (mat_x, mat_y, mat_z)
    squares = (mat_x * mat_x, mat_y * mat_y, mat_z * mat_z)
    weight_x = jnp.asarray(np.tile(weights, size_x // points), dtype=jnp.float32)
    weight_y = jnp.asarray(np.tile(weights, size_y // points), dtype=jnp.float32)
    weight_z = jnp.asarray(np.tile(weights, size_z // points), dtype=jnp.float32)
    scaled = (
        coefficient * weight_x[:, None, None] * weight_y[None, :, None] * weight_z[None, None, :]
    )
    diagonal = assemble(backward_sum((scaled, scaled, scaled), squares), points)
    inverse = 1.0 / diagonal
    theta = (eig_high + eig_low) / 2.0
    delta = (eig_high - eig_low) / 2.0
    sigma = theta / delta
    residual = right_side
    direction = inverse * residual / theta
    smoothed = direction
    rho = 1.0 / sigma
    for sweep in range(CHEB):
        grads = forward_parts(direction, mats)
        local = backward_sum((scaled * grads[0], scaled * grads[1], scaled * grads[2]), mats)
        residual = residual - assemble(local, points)
        if sweep + 1 < CHEB:
            rho_new = 1.0 / (2.0 * sigma - rho)
            direction = rho_new * rho * direction + 2.0 * rho_new / delta * inverse * residual
            smoothed = smoothed + direction
            rho = rho_new
    aggregates = coarse_factor.shape[0]
    column_sums = jnp.sum(agg_weight * residual, axis=(0, 1))
    coarse_rhs = jnp.sum(column_sums.reshape(aggregates, size_z // aggregates), axis=1)
    partial_term = jnp.dot(coarse_rhs, coarse_factor, precision=highest)
    projected = butterfly_sum(partial_term, ("gy", "gz", "gx"))
    coarse_solution = jnp.dot(coarse_factor, projected, precision=highest)
    spread = jnp.repeat(coarse_solution, size_z // aggregates)
    pressure_update = smoothed + agg_weight * spread[None, None, :]
    return (pressure_update, coarse_solution)


def solution(mesh):
    return jax.shard_map(
        per_device,
        mesh=mesh,
        in_specs=(
            P("gx", "gy", "gz"),
            P("gx", "gy", "gz"),
            P("gx", "gy", "gz"),
            P(("gx", "gy", "gz"), None),
        ),
        out_specs=(P("gx", "gy", "gz"), P(("gx", "gy", "gz"))),
        check_vma=False,
    )
```

```python
import jax
import jax.numpy as jnp
import numpy as np
from jax import lax
from jax.sharding import PartitionSpec as P

ORDER = 7
CHEB = 4


highest = lax.Precision.HIGHEST
eig_high = 4.0
eig_low = 0.2
gll_inner = np.array(
    [
        -0.8717401485096066,
        -0.5917001814331423,
        -0.20929921790247888,
        0.20929921790247888,
        0.5917001814331423,
        0.8717401485096066,
    ]
)


def padded_2(cells, sides, width):
    for axis, dim in sides:
        count = lax.axis_size(axis)
        ends = count - 1
        head = lax.slice_in_dim(cells, 0, width, axis=dim)
        tail = lax.slice_in_dim(cells, cells.shape[dim] - width, cells.shape[dim], axis=dim)
        from_prev = lax.ppermute(jnp.squeeze(tail, dim), axis, [(i, i + 1) for i in range(ends)])
        from_next = lax.ppermute(jnp.squeeze(head, dim), axis, [(i + 1, i) for i in range(ends)])
        cells = jnp.concatenate(
            [jnp.expand_dims(from_prev, dim), cells, jnp.expand_dims(from_next, dim)],
            axis=dim,
        )
    return cells


def exchange(value, axis, masks):
    count = lax.axis_size(axis)
    parts = [lax.ppermute(value, axis, [(i, i ^ mask) for i in range(count)]) for mask in masks]
    for part in parts:
        value = value + part
    return value


def butterfly_sum(value, axes):
    for axis in axes:
        count = lax.axis_size(axis)
        stride = 1
        while stride < count:
            if count == 4 * stride and count >= 32:
                value = exchange(value, axis, [stride, 2 * stride, 3 * stride])
                stride *= 4
            else:
                value = exchange(value, axis, [stride])
                stride *= 2
    return value


def legendre_value(nodes, degree):
    previous = nodes * 0.0 + 1.0
    current = nodes
    for step in range(1, degree):
        following = ((2.0 * step + 1.0) * nodes * current - step * previous) / (step + 1.0)
        previous = current
        current = following
    return current


def gll_tables(poly_order):
    point_count = poly_order + 1
    gll_nodes = np.concatenate([np.array([-1.0]), gll_inner, np.array([1.0])])
    at_nodes = legendre_value(gll_nodes, poly_order)
    weights = 2.0 / (poly_order * point_count * at_nodes**2)
    differences = gll_nodes[:, None] - gll_nodes[None, :] + np.eye(point_count)
    derivative = at_nodes[:, None] / (at_nodes[None, :] * differences) * (1.0 - np.eye(point_count))
    end_value = poly_order * point_count / 4.0
    end_row = np.concatenate(
        [np.array([-end_value]), np.zeros(poly_order - 1), np.array([end_value])]
    )
    derivative = derivative + np.eye(point_count) * end_row[None, :]
    return (derivative, weights)


def forward_parts(field, mats):
    mat_x, mat_y, mat_z = mats
    size_x, size_y, size_z = field.shape
    grad_x = jnp.einsum("ia,ajk->ijk", mat_x, field, precision=highest)
    grad_y = jnp.einsum("ja,iak->ijk", mat_y, field, precision=highest)
    blocks = field.reshape(size_x, size_y, size_z // 128, 128)
    grad_z = jnp.einsum("ca,ijsa->ijsc", mat_z, blocks, precision=highest).reshape(field.shape)
    return (grad_x, grad_y, grad_z)


def backward_sum(parts, mats):
    mat_x, mat_y, mat_z = mats
    part_x, part_y, part_z = parts
    size_x, size_y, size_z = part_x.shape
    total = jnp.einsum("ai,ajk->ijk", mat_x, part_x, precision=highest)
    total = total + jnp.einsum("aj,iak->ijk", mat_y, part_y, precision=highest)
    blocks = part_z.reshape(size_x, size_y, size_z // 128, 128)
    total = total + jnp.einsum("ac,ijsa->ijsc", mat_z, blocks, precision=highest).reshape(
        part_x.shape
    )
    return total


def combine(padded, axis_dim, length, points):
    own = lax.slice_in_dim(padded, 1, length + 1, axis=axis_dim)
    left = lax.slice_in_dim(padded, 0, length, axis=axis_dim)
    right = lax.slice_in_dim(padded, 2, length + 2, axis=axis_dim)
    shape_list = [1, 1, 1]
    shape_list[axis_dim] = length
    position = (jnp.arange(length, dtype=jnp.int32) % points).reshape(shape_list)
    low_mask = (position == 0).astype(jnp.float32)
    high_mask = (position == points - 1).astype(jnp.float32)
    return own + low_mask * left + high_mask * right


def assemble(field, points):
    size_x, size_y, size_z = field.shape
    padded = padded_2(field, (("gz", 2), ("gy", 1), ("gx", 0)), 1)
    summed = combine(padded, 0, size_x, points)
    summed = combine(summed, 1, size_y, points)
    summed = combine(summed, 2, size_z, points)
    return summed


def per_device(right_side, coefficient, agg_weight, coarse_factor):
    points = ORDER + 1
    derivative, weights = gll_tables(ORDER)
    size_x, size_y, size_z = right_side.shape
    mat_x = jnp.asarray(np.kron(np.eye(size_x // points), derivative), dtype=jnp.float32)
    mat_y = jnp.asarray(np.kron(np.eye(size_y // points), derivative), dtype=jnp.float32)
    mat_z = jnp.asarray(np.kron(np.eye(128 // points), derivative), dtype=jnp.float32)
    mats = (mat_x, mat_y, mat_z)
    squares = (mat_x * mat_x, mat_y * mat_y, mat_z * mat_z)
    weight_x = jnp.asarray(np.tile(weights, size_x // points), dtype=jnp.float32)
    weight_y = jnp.asarray(np.tile(weights, size_y // points), dtype=jnp.float32)
    weight_z = jnp.asarray(np.tile(weights, size_z // points), dtype=jnp.float32)
    scaled = (
        coefficient * weight_x[:, None, None] * weight_y[None, :, None] * weight_z[None, None, :]
    )
    diagonal = assemble(backward_sum((scaled, scaled, scaled), squares), points)
    inverse = 1.0 / diagonal
    theta = (eig_high + eig_low) / 2.0
    delta = (eig_high - eig_low) / 2.0
    sigma = theta / delta
    residual = right_side
    direction = inverse * residual / theta
    smoothed = direction
    rho = 1.0 / sigma
    for sweep in range(CHEB):
        grads = forward_parts(direction, mats)
        local = backward_sum((scaled * grads[0], scaled * grads[1], scaled * grads[2]), mats)
        residual = residual - assemble(local, points)
        if sweep + 1 < CHEB:
            rho_new = 1.0 / (2.0 * sigma - rho)
            direction = rho_new * rho * direction + 2.0 * rho_new / delta * inverse * residual
            smoothed = smoothed + direction
            rho = rho_new
    aggregates = coarse_factor.shape[0]
    column_sums = jnp.sum(agg_weight * residual, axis=(0, 1))
    coarse_rhs = jnp.sum(column_sums.reshape(aggregates, size_z // aggregates), axis=1)
    partial_term = jnp.dot(coarse_rhs, coarse_factor, precision=highest)
    projected = butterfly_sum(partial_term, ("gy", "gz", "gx"))
    coarse_solution = jnp.dot(coarse_factor, projected, precision=highest)
    spread = jnp.repeat(coarse_solution, size_z // aggregates)
    pressure_update = smoothed + agg_weight * spread[None, None, :]
    return (pressure_update, coarse_solution)


def solution(mesh):
    return jax.shard_map(
        per_device,
        mesh=mesh,
        in_specs=(
            P("gx", "gy", "gz"),
            P("gx", "gy", "gz"),
            P("gx", "gy", "gz"),
            P(("gx", "gy", "gz"), None),
        ),
        out_specs=(P("gx", "gy", "gz"), P(("gx", "gy", "gz"))),
        check_vma=False,
    )
```

```python
import jax
import jax.numpy as jnp
import numpy as np
from jax import lax
from jax.sharding import PartitionSpec as P

ORDER = 7
CHEB = 4


highest = lax.Precision.HIGHEST
eig_high = 4.0
eig_low = 0.2
gll_inner = np.array(
    [
        -0.8717401485096066,
        -0.5917001814331423,
        -0.20929921790247888,
        0.20929921790247888,
        0.5917001814331423,
        0.8717401485096066,
    ]
)


def padded_2(cells, sides, width):
    for axis, dim in sides:
        count = lax.axis_size(axis)
        ends = count - 1
        head = lax.slice_in_dim(cells, 0, width, axis=dim)
        tail = lax.slice_in_dim(cells, cells.shape[dim] - width, cells.shape[dim], axis=dim)
        from_prev = lax.ppermute(jnp.squeeze(tail, dim), axis, [(i, i + 1) for i in range(ends)])
        from_next = lax.ppermute(jnp.squeeze(head, dim), axis, [(i + 1, i) for i in range(ends)])
        cells = jnp.concatenate(
            [jnp.expand_dims(from_prev, dim), cells, jnp.expand_dims(from_next, dim)],
            axis=dim,
        )
    return cells


def group_partner(index, size, pairing):
    group = index // size
    return index + (pairing(group) - group) * size


def butterfly_sum(value, axes):
    for axis in axes:
        count = lax.axis_size(axis)
        size = count // 4
        stride = 1
        while stride < size:
            value = value + lax.ppermute(value, axis, [(i, i ^ stride) for i in range(count)])
            stride *= 2
        for pairing in (lambda g: 3 - g, lambda g: g ^ 1):
            pairs = [(i, group_partner(i, size, pairing)) for i in range(count)]
            value = value + lax.ppermute(value, axis, pairs)
    return value


def legendre_value(nodes, degree):
    previous = nodes * 0.0 + 1.0
    current = nodes
    for step in range(1, degree):
        following = ((2.0 * step + 1.0) * nodes * current - step * previous) / (step + 1.0)
        previous = current
        current = following
    return current


def gll_tables(poly_order):
    point_count = poly_order + 1
    gll_nodes = np.concatenate([np.array([-1.0]), gll_inner, np.array([1.0])])
    at_nodes = legendre_value(gll_nodes, poly_order)
    weights = 2.0 / (poly_order * point_count * at_nodes**2)
    differences = gll_nodes[:, None] - gll_nodes[None, :] + np.eye(point_count)
    derivative = at_nodes[:, None] / (at_nodes[None, :] * differences) * (1.0 - np.eye(point_count))
    end_value = poly_order * point_count / 4.0
    end_row = np.concatenate(
        [np.array([-end_value]), np.zeros(poly_order - 1), np.array([end_value])]
    )
    derivative = derivative + np.eye(point_count) * end_row[None, :]
    return (derivative, weights)


def forward_parts(field, mats):
    mat_x, mat_y, mat_z = mats
    size_x, size_y, size_z = field.shape
    grad_x = jnp.einsum("ia,ajk->ijk", mat_x, field, precision=highest)
    grad_y = jnp.einsum("ja,iak->ijk", mat_y, field, precision=highest)
    blocks = field.reshape(size_x, size_y, size_z // 128, 128)
    grad_z = jnp.einsum("ca,ijsa->ijsc", mat_z, blocks, precision=highest).reshape(field.shape)
    return (grad_x, grad_y, grad_z)


def backward_sum(parts, mats):
    mat_x, mat_y, mat_z = mats
    part_x, part_y, part_z = parts
    size_x, size_y, size_z = part_x.shape
    total = jnp.einsum("ai,ajk->ijk", mat_x, part_x, precision=highest)
    total = total + jnp.einsum("aj,iak->ijk", mat_y, part_y, precision=highest)
    blocks = part_z.reshape(size_x, size_y, size_z // 128, 128)
    total = total + jnp.einsum("ac,ijsa->ijsc", mat_z, blocks, precision=highest).reshape(
        part_x.shape
    )
    return total


def combine(padded, axis_dim, length, points):
    own = lax.slice_in_dim(padded, 1, length + 1, axis=axis_dim)
    left = lax.slice_in_dim(padded, 0, length, axis=axis_dim)
    right = lax.slice_in_dim(padded, 2, length + 2, axis=axis_dim)
    shape_list = [1, 1, 1]
    shape_list[axis_dim] = length
    position = (jnp.arange(length, dtype=jnp.int32) % points).reshape(shape_list)
    low_mask = (position == 0).astype(jnp.float32)
    high_mask = (position == points - 1).astype(jnp.float32)
    return own + low_mask * left + high_mask * right


def assemble(field, points):
    size_x, size_y, size_z = field.shape
    padded = padded_2(field, (("gz", 2), ("gy", 1), ("gx", 0)), 1)
    summed = combine(padded, 0, size_x, points)
    summed = combine(summed, 1, size_y, points)
    summed = combine(summed, 2, size_z, points)
    return summed


def per_device(right_side, coefficient, agg_weight, coarse_factor):
    points = ORDER + 1
    derivative, weights = gll_tables(ORDER)
    size_x, size_y, size_z = right_side.shape
    mat_x = jnp.asarray(np.kron(np.eye(size_x // points), derivative), dtype=jnp.float32)
    mat_y = jnp.asarray(np.kron(np.eye(size_y // points), derivative), dtype=jnp.float32)
    mat_z = jnp.asarray(np.kron(np.eye(128 // points), derivative), dtype=jnp.float32)
    mats = (mat_x, mat_y, mat_z)
    squares = (mat_x * mat_x, mat_y * mat_y, mat_z * mat_z)
    weight_x = jnp.asarray(np.tile(weights, size_x // points), dtype=jnp.float32)
    weight_y = jnp.asarray(np.tile(weights, size_y // points), dtype=jnp.float32)
    weight_z = jnp.asarray(np.tile(weights, size_z // points), dtype=jnp.float32)
    scaled = (
        coefficient * weight_x[:, None, None] * weight_y[None, :, None] * weight_z[None, None, :]
    )
    diagonal = assemble(backward_sum((scaled, scaled, scaled), squares), points)
    inverse = 1.0 / diagonal
    theta = (eig_high + eig_low) / 2.0
    delta = (eig_high - eig_low) / 2.0
    sigma = theta / delta
    residual = right_side
    direction = inverse * residual / theta
    smoothed = direction
    rho = 1.0 / sigma
    for sweep in range(CHEB):
        grads = forward_parts(direction, mats)
        local = backward_sum((scaled * grads[0], scaled * grads[1], scaled * grads[2]), mats)
        residual = residual - assemble(local, points)
        if sweep + 1 < CHEB:
            rho_new = 1.0 / (2.0 * sigma - rho)
            direction = rho_new * rho * direction + 2.0 * rho_new / delta * inverse * residual
            smoothed = smoothed + direction
            rho = rho_new
    aggregates = coarse_factor.shape[0]
    column_sums = jnp.sum(agg_weight * residual, axis=(0, 1))
    coarse_rhs = jnp.sum(column_sums.reshape(aggregates, size_z // aggregates), axis=1)
    partial_term = jnp.dot(coarse_rhs, coarse_factor, precision=highest)
    projected = butterfly_sum(partial_term, ("gy", "gz", "gx"))
    coarse_solution = jnp.dot(coarse_factor, projected, precision=highest)
    spread = jnp.repeat(coarse_solution, size_z // aggregates)
    pressure_update = smoothed + agg_weight * spread[None, None, :]
    return (pressure_update, coarse_solution)


def solution(mesh):
    return jax.shard_map(
        per_device,
        mesh=mesh,
        in_specs=(
            P("gx", "gy", "gz"),
            P("gx", "gy", "gz"),
            P("gx", "gy", "gz"),
            P(("gx", "gy", "gz"), None),
        ),
        out_specs=(P("gx", "gy", "gz"), P(("gx", "gy", "gz"))),
        check_vma=False,
    )
```

```python
import jax
import jax.numpy as jnp
import numpy as np
from jax import lax
from jax.sharding import PartitionSpec as P

ORDER = 7
CHEB = 4


highest = lax.Precision.HIGHEST
eig_high = 4.0
eig_low = 0.2
gll_inner = np.array(
    [
        -0.8717401485096066,
        -0.5917001814331423,
        -0.20929921790247888,
        0.20929921790247888,
        0.5917001814331423,
        0.8717401485096066,
    ]
)


def padded_2(cells, sides, width):
    for axis, dim in sides:
        count = lax.axis_size(axis)
        ends = count - 1
        head = lax.slice_in_dim(cells, 0, width, axis=dim)
        tail = lax.slice_in_dim(cells, cells.shape[dim] - width, cells.shape[dim], axis=dim)
        from_prev = lax.ppermute(jnp.squeeze(tail, dim), axis, [(i, i + 1) for i in range(ends)])
        from_next = lax.ppermute(jnp.squeeze(head, dim), axis, [(i + 1, i) for i in range(ends)])
        cells = jnp.concatenate(
            [jnp.expand_dims(from_prev, dim), cells, jnp.expand_dims(from_next, dim)],
            axis=dim,
        )
    return cells


def group_partner(index, size, pairing):
    group = index // size
    return index + (pairing(group) - group) * size


def butterfly_sum(value, axes):
    for axis in axes:
        count = lax.axis_size(axis)
        size = count // 4
        stride = 1
        while stride < size:
            value = value + lax.ppermute(value, axis, [(i, i ^ stride) for i in range(count)])
            stride *= 2
        for pairing in (lambda g: 3 - g, lambda g: g ^ 1):
            pairs = [(i, group_partner(i, size, pairing)) for i in range(count)]
            value = value + lax.ppermute(value, axis, pairs)
    return value


def legendre_value(nodes, degree):
    previous = nodes * 0.0 + 1.0
    current = nodes
    for step in range(1, degree):
        following = ((2.0 * step + 1.0) * nodes * current - step * previous) / (step + 1.0)
        previous = current
        current = following
    return current


def gll_tables(poly_order):
    point_count = poly_order + 1
    gll_nodes = np.concatenate([np.array([-1.0]), gll_inner, np.array([1.0])])
    at_nodes = legendre_value(gll_nodes, poly_order)
    weights = 2.0 / (poly_order * point_count * at_nodes**2)
    differences = gll_nodes[:, None] - gll_nodes[None, :] + np.eye(point_count)
    derivative = at_nodes[:, None] / (at_nodes[None, :] * differences) * (1.0 - np.eye(point_count))
    end_value = poly_order * point_count / 4.0
    end_row = np.concatenate(
        [np.array([-end_value]), np.zeros(poly_order - 1), np.array([end_value])]
    )
    derivative = derivative + np.eye(point_count) * end_row[None, :]
    return (derivative, weights)


def forward_parts(field, mats):
    mat_x, mat_y, mat_z = mats
    size_x, size_y, size_z = field.shape
    grad_x = jnp.einsum("ia,ajk->ijk", mat_x, field, precision=highest)
    grad_y = jnp.einsum("ja,iak->ijk", mat_y, field, precision=highest)
    blocks = field.reshape(size_x, size_y, size_z // 128, 128)
    grad_z = jnp.einsum("ca,ijsa->ijsc", mat_z, blocks, precision=highest).reshape(field.shape)
    return (grad_x, grad_y, grad_z)


def backward_sum(parts, mats):
    mat_x, mat_y, mat_z = mats
    part_x, part_y, part_z = parts
    size_x, size_y, size_z = part_x.shape
    total = jnp.einsum("ai,ajk->ijk", mat_x, part_x, precision=highest)
    total = total + jnp.einsum("aj,iak->ijk", mat_y, part_y, precision=highest)
    blocks = part_z.reshape(size_x, size_y, size_z // 128, 128)
    total = total + jnp.einsum("ac,ijsa->ijsc", mat_z, blocks, precision=highest).reshape(
        part_x.shape
    )
    return total


def combine(padded, axis_dim, length, points):
    own = lax.slice_in_dim(padded, 1, length + 1, axis=axis_dim)
    left = lax.slice_in_dim(padded, 0, length, axis=axis_dim)
    right = lax.slice_in_dim(padded, 2, length + 2, axis=axis_dim)
    shape_list = [1, 1, 1]
    shape_list[axis_dim] = length
    position = (jnp.arange(length, dtype=jnp.int32) % points).reshape(shape_list)
    low_mask = (position == 0).astype(jnp.float32)
    high_mask = (position == points - 1).astype(jnp.float32)
    return own + low_mask * left + high_mask * right


def ghost_z(cells, width):
    count = lax.axis_size("gz")
    head = cells[..., :width]
    tail = cells[..., cells.shape[-1] - width :]
    from_prev = lax.ppermute(tail, "gz", [(i, i + 1) for i in range(count - 1)])
    from_next = lax.ppermute(head, "gz", [(i + 1, i) for i in range(count - 1)])
    return jnp.concatenate([from_prev, cells, from_next], axis=-1)


def assemble(field, points):
    size_x, size_y, size_z = field.shape
    padded = jnp.pad(field, ((0, 0), (0, 0), (1, 1)))
    padded = padded_2(padded, (("gy", 1), ("gx", 0)), 1)
    summed = combine(padded, 0, size_x, points)
    summed = combine(summed, 1, size_y, points)
    summed = combine(summed, 2, size_z, points)
    return summed


def per_device(right_side, coefficient, agg_weight, coarse_factor):
    points = ORDER + 1
    derivative, weights = gll_tables(ORDER)
    size_x, size_y, own_z = right_side.shape
    ghost = 64
    inputs = ghost_z(jnp.stack([right_side, coefficient]), ghost)
    right_ext, coefficient = inputs[0], inputs[1]
    size_z = own_z + 2 * ghost
    first = lax.axis_index("gz") * own_z - ghost
    global_z = first + jnp.arange(size_z, dtype=jnp.int32)
    inside = ((global_z >= 0) & (global_z < own_z * lax.axis_size("gz")))[None, None, :]
    mat_x = jnp.asarray(np.kron(np.eye(size_x // points), derivative), dtype=jnp.float32)
    mat_y = jnp.asarray(np.kron(np.eye(size_y // points), derivative), dtype=jnp.float32)
    mat_z = jnp.asarray(np.kron(np.eye(128 // points), derivative), dtype=jnp.float32)
    mats = (mat_x, mat_y, mat_z)
    squares = (mat_x * mat_x, mat_y * mat_y, mat_z * mat_z)
    weight_x = jnp.asarray(np.tile(weights, size_x // points), dtype=jnp.float32)
    weight_y = jnp.asarray(np.tile(weights, size_y // points), dtype=jnp.float32)
    weight_z = jnp.asarray(np.tile(weights, size_z // points), dtype=jnp.float32)
    scaled = (
        coefficient * weight_x[:, None, None] * weight_y[None, :, None] * weight_z[None, None, :]
    )
    diagonal = assemble(backward_sum((scaled, scaled, scaled), squares), points)
    inverse = jnp.where(inside, 1.0 / diagonal, 0.0)
    theta = (eig_high + eig_low) / 2.0
    delta = (eig_high - eig_low) / 2.0
    sigma = theta / delta
    residual = right_ext
    direction = inverse * residual / theta
    smoothed = direction
    rho = 1.0 / sigma
    for sweep in range(CHEB):
        grads = forward_parts(direction, mats)
        local = backward_sum((scaled * grads[0], scaled * grads[1], scaled * grads[2]), mats)
        residual = residual - assemble(local, points)
        if sweep + 1 < CHEB:
            rho_new = 1.0 / (2.0 * sigma - rho)
            direction = rho_new * rho * direction + 2.0 * rho_new / delta * inverse * residual
            smoothed = smoothed + direction
            rho = rho_new
    residual = residual[:, :, ghost : ghost + own_z]
    smoothed = smoothed[:, :, ghost : ghost + own_z]
    size_z = own_z
    aggregates = coarse_factor.shape[0]
    column_sums = jnp.sum(agg_weight * residual, axis=(0, 1))
    coarse_rhs = jnp.sum(column_sums.reshape(aggregates, size_z // aggregates), axis=1)
    partial_term = jnp.dot(coarse_rhs, coarse_factor, precision=highest)
    projected = butterfly_sum(partial_term, ("gy", "gz", "gx"))
    coarse_solution = jnp.dot(coarse_factor, projected, precision=highest)
    spread = jnp.repeat(coarse_solution, size_z // aggregates)
    pressure_update = smoothed + agg_weight * spread[None, None, :]
    return (pressure_update, coarse_solution)


def solution(mesh):
    return jax.shard_map(
        per_device,
        mesh=mesh,
        in_specs=(
            P("gx", "gy", "gz"),
            P("gx", "gy", "gz"),
            P("gx", "gy", "gz"),
            P(("gx", "gy", "gz"), None),
        ),
        out_specs=(P("gx", "gy", "gz"), P(("gx", "gy", "gz"))),
        check_vma=False,
    )
```

```python
import jax
import jax.numpy as jnp
import numpy as np
from jax import lax
from jax.sharding import PartitionSpec as P

ORDER = 7
CHEB = 4


highest = lax.Precision.HIGHEST
local_precision = lax.Precision.HIGH
eig_high = 4.0
eig_low = 0.2
gll_inner = np.array(
    [
        -0.8717401485096066,
        -0.5917001814331423,
        -0.20929921790247888,
        0.20929921790247888,
        0.5917001814331423,
        0.8717401485096066,
    ]
)


def padded_2(cells, sides, width):
    for axis, dim in sides:
        count = lax.axis_size(axis)
        ends = count - 1
        head = lax.slice_in_dim(cells, 0, width, axis=dim)
        tail = lax.slice_in_dim(cells, cells.shape[dim] - width, cells.shape[dim], axis=dim)
        from_prev = lax.ppermute(jnp.squeeze(tail, dim), axis, [(i, i + 1) for i in range(ends)])
        from_next = lax.ppermute(jnp.squeeze(head, dim), axis, [(i + 1, i) for i in range(ends)])
        cells = jnp.concatenate(
            [jnp.expand_dims(from_prev, dim), cells, jnp.expand_dims(from_next, dim)],
            axis=dim,
        )
    return cells


def group_partner(index, size, pairing):
    group = index // size
    return index + (pairing(group) - group) * size


def butterfly_sum(value, axes):
    for axis in axes:
        count = lax.axis_size(axis)
        size = count // 4
        stride = 1
        while stride < size:
            value = value + lax.ppermute(value, axis, [(i, i ^ stride) for i in range(count)])
            stride *= 2
        for pairing in (lambda g: 3 - g, lambda g: g ^ 1):
            pairs = [(i, group_partner(i, size, pairing)) for i in range(count)]
            value = value + lax.ppermute(value, axis, pairs)
    return value


def legendre_value(nodes, degree):
    previous = nodes * 0.0 + 1.0
    current = nodes
    for step in range(1, degree):
        following = ((2.0 * step + 1.0) * nodes * current - step * previous) / (step + 1.0)
        previous = current
        current = following
    return current


def gll_tables(poly_order):
    point_count = poly_order + 1
    gll_nodes = np.concatenate([np.array([-1.0]), gll_inner, np.array([1.0])])
    at_nodes = legendre_value(gll_nodes, poly_order)
    weights = 2.0 / (poly_order * point_count * at_nodes**2)
    differences = gll_nodes[:, None] - gll_nodes[None, :] + np.eye(point_count)
    derivative = at_nodes[:, None] / (at_nodes[None, :] * differences) * (1.0 - np.eye(point_count))
    end_value = poly_order * point_count / 4.0
    end_row = np.concatenate(
        [np.array([-end_value]), np.zeros(poly_order - 1), np.array([end_value])]
    )
    derivative = derivative + np.eye(point_count) * end_row[None, :]
    return (derivative, weights)


def forward_parts(field, mats):
    mat_x, mat_y, mat_z = mats
    size_x, size_y, size_z = field.shape
    grad_x = jnp.einsum("ia,ajk->ijk", mat_x, field, precision=local_precision)
    grad_y = jnp.einsum("ja,iak->ijk", mat_y, field, precision=local_precision)
    blocks = field.reshape(size_x, size_y, size_z // 128, 128)
    grad_z = jnp.einsum("ca,ijsa->ijsc", mat_z, blocks, precision=local_precision).reshape(field.shape)
    return (grad_x, grad_y, grad_z)


def backward_sum(parts, mats):
    mat_x, mat_y, mat_z = mats
    part_x, part_y, part_z = parts
    size_x, size_y, size_z = part_x.shape
    total = jnp.einsum("ai,ajk->ijk", mat_x, part_x, precision=local_precision)
    total = total + jnp.einsum("aj,iak->ijk", mat_y, part_y, precision=local_precision)
    blocks = part_z.reshape(size_x, size_y, size_z // 128, 128)
    total = total + jnp.einsum("ac,ijsa->ijsc", mat_z, blocks, precision=local_precision).reshape(
        part_x.shape
    )
    return total


def combine(padded, axis_dim, length, points):
    own = lax.slice_in_dim(padded, 1, length + 1, axis=axis_dim)
    left = lax.slice_in_dim(padded, 0, length, axis=axis_dim)
    right = lax.slice_in_dim(padded, 2, length + 2, axis=axis_dim)
    shape_list = [1, 1, 1]
    shape_list[axis_dim] = length
    position = (jnp.arange(length, dtype=jnp.int32) % points).reshape(shape_list)
    low_mask = (position == 0).astype(jnp.float32)
    high_mask = (position == points - 1).astype(jnp.float32)
    return own + low_mask * left + high_mask * right


def ghost_z(cells, width):
    count = lax.axis_size("gz")
    head = cells[..., :width]
    tail = cells[..., cells.shape[-1] - width :]
    from_prev = lax.ppermute(tail, "gz", [(i, i + 1) for i in range(count - 1)])
    from_next = lax.ppermute(head, "gz", [(i + 1, i) for i in range(count - 1)])
    return jnp.concatenate([from_prev, cells, from_next], axis=-1)


def assemble(field, points):
    size_x, size_y, size_z = field.shape
    padded = jnp.pad(field, ((0, 0), (0, 0), (1, 1)))
    padded = padded_2(padded, (("gy", 1), ("gx", 0)), 1)
    summed = combine(padded, 0, size_x, points)
    summed = combine(summed, 1, size_y, points)
    summed = combine(summed, 2, size_z, points)
    return summed


def per_device(right_side, coefficient, agg_weight, coarse_factor):
    points = ORDER + 1
    derivative, weights = gll_tables(ORDER)
    size_x, size_y, own_z = right_side.shape
    ghost = 64
    inputs = ghost_z(jnp.stack([right_side, coefficient]), ghost)
    right_ext, coefficient = inputs[0], inputs[1]
    size_z = own_z + 2 * ghost
    first = lax.axis_index("gz") * own_z - ghost
    global_z = first + jnp.arange(size_z, dtype=jnp.int32)
    inside = ((global_z >= 0) & (global_z < own_z * lax.axis_size("gz")))[None, None, :]
    mat_x = jnp.asarray(np.kron(np.eye(size_x // points), derivative), dtype=jnp.float32)
    mat_y = jnp.asarray(np.kron(np.eye(size_y // points), derivative), dtype=jnp.float32)
    mat_z = jnp.asarray(np.kron(np.eye(128 // points), derivative), dtype=jnp.float32)
    mats = (mat_x, mat_y, mat_z)
    squares = (mat_x * mat_x, mat_y * mat_y, mat_z * mat_z)
    weight_x = jnp.asarray(np.tile(weights, size_x // points), dtype=jnp.float32)
    weight_y = jnp.asarray(np.tile(weights, size_y // points), dtype=jnp.float32)
    weight_z = jnp.asarray(np.tile(weights, size_z // points), dtype=jnp.float32)
    scaled = (
        coefficient * weight_x[:, None, None] * weight_y[None, :, None] * weight_z[None, None, :]
    )
    diagonal = assemble(backward_sum((scaled, scaled, scaled), squares), points)
    inverse = jnp.where(inside, 1.0 / diagonal, 0.0)
    theta = (eig_high + eig_low) / 2.0
    delta = (eig_high - eig_low) / 2.0
    sigma = theta / delta
    residual = right_ext
    direction = inverse * residual / theta
    smoothed = direction
    rho = 1.0 / sigma
    for sweep in range(CHEB):
        grads = forward_parts(direction, mats)
        local = backward_sum((scaled * grads[0], scaled * grads[1], scaled * grads[2]), mats)
        residual = residual - assemble(local, points)
        if sweep + 1 < CHEB:
            rho_new = 1.0 / (2.0 * sigma - rho)
            direction = rho_new * rho * direction + 2.0 * rho_new / delta * inverse * residual
            smoothed = smoothed + direction
            rho = rho_new
    residual = residual[:, :, ghost : ghost + own_z]
    smoothed = smoothed[:, :, ghost : ghost + own_z]
    size_z = own_z
    aggregates = coarse_factor.shape[0]
    column_sums = jnp.sum(agg_weight * residual, axis=(0, 1))
    coarse_rhs = jnp.sum(column_sums.reshape(aggregates, size_z // aggregates), axis=1)
    partial_term = jnp.dot(coarse_rhs, coarse_factor, precision=highest)
    projected = butterfly_sum(partial_term, ("gy", "gz", "gx"))
    coarse_solution = jnp.dot(coarse_factor, projected, precision=highest)
    spread = jnp.repeat(coarse_solution, size_z // aggregates)
    pressure_update = smoothed + agg_weight * spread[None, None, :]
    return (pressure_update, coarse_solution)


def solution(mesh):
    return jax.shard_map(
        per_device,
        mesh=mesh,
        in_specs=(
            P("gx", "gy", "gz"),
            P("gx", "gy", "gz"),
            P("gx", "gy", "gz"),
            P(("gx", "gy", "gz"), None),
        ),
        out_specs=(P("gx", "gy", "gz"), P(("gx", "gy", "gz"))),
        check_vma=False,
    )
```

```python
import jax
import jax.numpy as jnp
import numpy as np
from jax import lax
from jax.sharding import PartitionSpec as P

ORDER = 7
CHEB = 4


highest = lax.Precision.HIGHEST
local_precision = lax.Precision.HIGH
eig_high = 4.0
eig_low = 0.2
gll_inner = np.array(
    [
        -0.8717401485096066,
        -0.5917001814331423,
        -0.20929921790247888,
        0.20929921790247888,
        0.5917001814331423,
        0.8717401485096066,
    ]
)


def padded_2(cells, sides, width):
    for axis, dim in sides:
        count = lax.axis_size(axis)
        ends = count - 1
        head = lax.slice_in_dim(cells, 0, width, axis=dim)
        tail = lax.slice_in_dim(cells, cells.shape[dim] - width, cells.shape[dim], axis=dim)
        from_prev = lax.ppermute(jnp.squeeze(tail, dim), axis, [(i, i + 1) for i in range(ends)])
        from_next = lax.ppermute(jnp.squeeze(head, dim), axis, [(i + 1, i) for i in range(ends)])
        cells = jnp.concatenate(
            [jnp.expand_dims(from_prev, dim), cells, jnp.expand_dims(from_next, dim)],
            axis=dim,
        )
    return cells


def group_partner(index, size, pairing):
    group = index // size
    return index + (pairing(group) - group) * size


def butterfly_sum(value, axes):
    for axis in axes:
        count = lax.axis_size(axis)
        size = count // 4
        stride = 1
        while stride < size:
            value = value + lax.ppermute(value, axis, [(i, i ^ stride) for i in range(count)])
            stride *= 2
        for pairing in (lambda g: 3 - g, lambda g: g ^ 1):
            pairs = [(i, group_partner(i, size, pairing)) for i in range(count)]
            value = value + lax.ppermute(value, axis, pairs)
    return value


def legendre_value(nodes, degree):
    previous = nodes * 0.0 + 1.0
    current = nodes
    for step in range(1, degree):
        following = ((2.0 * step + 1.0) * nodes * current - step * previous) / (step + 1.0)
        previous = current
        current = following
    return current


def gll_tables(poly_order):
    point_count = poly_order + 1
    gll_nodes = np.concatenate([np.array([-1.0]), gll_inner, np.array([1.0])])
    at_nodes = legendre_value(gll_nodes, poly_order)
    weights = 2.0 / (poly_order * point_count * at_nodes**2)
    differences = gll_nodes[:, None] - gll_nodes[None, :] + np.eye(point_count)
    derivative = at_nodes[:, None] / (at_nodes[None, :] * differences) * (1.0 - np.eye(point_count))
    end_value = poly_order * point_count / 4.0
    end_row = np.concatenate(
        [np.array([-end_value]), np.zeros(poly_order - 1), np.array([end_value])]
    )
    derivative = derivative + np.eye(point_count) * end_row[None, :]
    return (derivative, weights)


def forward_parts(field, mats):
    mat_x, mat_y, mat_z = mats
    size_x, size_y, size_z = field.shape
    grad_x = jnp.einsum("ia,ajk->ijk", mat_x, field, precision=local_precision)
    grad_y = jnp.einsum("ja,iak->ijk", mat_y, field, precision=local_precision)
    blocks = field.reshape(size_x, size_y, size_z // 128, 128)
    grad_z = jnp.einsum("ca,ijsa->ijsc", mat_z, blocks, precision=local_precision).reshape(field.shape)
    return (grad_x, grad_y, grad_z)


def backward_sum(parts, mats):
    mat_x, mat_y, mat_z = mats
    part_x, part_y, part_z = parts
    size_x, size_y, size_z = part_x.shape
    total = jnp.einsum("ai,ajk->ijk", mat_x, part_x, precision=local_precision)
    total = total + jnp.einsum("aj,iak->ijk", mat_y, part_y, precision=local_precision)
    blocks = part_z.reshape(size_x, size_y, size_z // 128, 128)
    total = total + jnp.einsum("ac,ijsa->ijsc", mat_z, blocks, precision=local_precision).reshape(
        part_x.shape
    )
    return total


def combine(padded, axis_dim, length, points):
    own = lax.slice_in_dim(padded, 1, length + 1, axis=axis_dim)
    left = lax.slice_in_dim(padded, 0, length, axis=axis_dim)
    right = lax.slice_in_dim(padded, 2, length + 2, axis=axis_dim)
    shape_list = [1, 1, 1]
    shape_list[axis_dim] = length
    position = (jnp.arange(length, dtype=jnp.int32) % points).reshape(shape_list)
    low_mask = (position == 0).astype(jnp.float32)
    high_mask = (position == points - 1).astype(jnp.float32)
    return own + low_mask * left + high_mask * right


def ghost_z(arrays, width):
    count = lax.axis_size("gz")
    head = jnp.stack([cells[..., :width] for cells in arrays])
    tail = jnp.stack([cells[..., cells.shape[-1] - width :] for cells in arrays])
    from_prev = lax.ppermute(tail, "gz", [(i, i + 1) for i in range(count - 1)])
    from_next = lax.ppermute(head, "gz", [(i + 1, i) for i in range(count - 1)])
    return [
        jnp.concatenate([from_prev[k], cells, from_next[k]], axis=-1)
        for k, cells in enumerate(arrays)
    ]


def assemble(field, points):
    size_x, size_y, size_z = field.shape
    padded = jnp.pad(field, ((0, 0), (0, 0), (1, 1)))
    padded = padded_2(padded, (("gy", 1), ("gx", 0)), 1)
    summed = combine(padded, 0, size_x, points)
    summed = combine(summed, 1, size_y, points)
    summed = combine(summed, 2, size_z, points)
    return summed


def per_device(right_side, coefficient, agg_weight, coarse_factor):
    points = ORDER + 1
    derivative, weights = gll_tables(ORDER)
    size_x, size_y, own_z = right_side.shape
    ghost = 64
    right_ext, coefficient = ghost_z([right_side, coefficient], ghost)
    size_z = own_z + 2 * ghost
    first = lax.axis_index("gz") * own_z - ghost
    global_z = first + jnp.arange(size_z, dtype=jnp.int32)
    inside = ((global_z >= 0) & (global_z < own_z * lax.axis_size("gz")))[None, None, :]
    mat_x = jnp.asarray(np.kron(np.eye(size_x // points), derivative), dtype=jnp.float32)
    mat_y = jnp.asarray(np.kron(np.eye(size_y // points), derivative), dtype=jnp.float32)
    mat_z = jnp.asarray(np.kron(np.eye(128 // points), derivative), dtype=jnp.float32)
    mats = (mat_x, mat_y, mat_z)
    squares = (mat_x * mat_x, mat_y * mat_y, mat_z * mat_z)
    weight_x = jnp.asarray(np.tile(weights, size_x // points), dtype=jnp.float32)
    weight_y = jnp.asarray(np.tile(weights, size_y // points), dtype=jnp.float32)
    weight_z = jnp.asarray(np.tile(weights, size_z // points), dtype=jnp.float32)
    scaled = (
        coefficient * weight_x[:, None, None] * weight_y[None, :, None] * weight_z[None, None, :]
    )
    diagonal = assemble(backward_sum((scaled, scaled, scaled), squares), points)
    inverse = jnp.where(inside, 1.0 / diagonal, 0.0)
    theta = (eig_high + eig_low) / 2.0
    delta = (eig_high - eig_low) / 2.0
    sigma = theta / delta
    residual = right_ext
    direction = inverse * residual / theta
    smoothed = direction
    rho = 1.0 / sigma
    for sweep in range(CHEB):
        grads = forward_parts(direction, mats)
        local = backward_sum((scaled * grads[0], scaled * grads[1], scaled * grads[2]), mats)
        residual = residual - assemble(local, points)
        if sweep + 1 < CHEB:
            rho_new = 1.0 / (2.0 * sigma - rho)
            direction = rho_new * rho * direction + 2.0 * rho_new / delta * inverse * residual
            smoothed = smoothed + direction
            rho = rho_new
    residual = residual[:, :, ghost : ghost + own_z]
    smoothed = smoothed[:, :, ghost : ghost + own_z]
    size_z = own_z
    aggregates = coarse_factor.shape[0]
    column_sums = jnp.sum(agg_weight * residual, axis=(0, 1))
    coarse_rhs = jnp.sum(column_sums.reshape(aggregates, size_z // aggregates), axis=1)
    partial_term = jnp.dot(coarse_rhs, coarse_factor, precision=highest)
    projected = butterfly_sum(partial_term, ("gy", "gz", "gx"))
    coarse_solution = jnp.dot(coarse_factor, projected, precision=highest)
    spread = jnp.repeat(coarse_solution, size_z // aggregates)
    pressure_update = smoothed + agg_weight * spread[None, None, :]
    return (pressure_update, coarse_solution)


def solution(mesh):
    return jax.shard_map(
        per_device,
        mesh=mesh,
        in_specs=(
            P("gx", "gy", "gz"),
            P("gx", "gy", "gz"),
            P("gx", "gy", "gz"),
            P(("gx", "gy", "gz"), None),
        ),
        out_specs=(P("gx", "gy", "gz"), P(("gx", "gy", "gz"))),
        check_vma=False,
    )
```

```python
import jax
import jax.numpy as jnp
import numpy as np
from jax import lax
from jax.sharding import PartitionSpec as P

ORDER = 7
CHEB = 4


highest = lax.Precision.HIGHEST
local_precision = lax.Precision.HIGH
eig_high = 4.0
eig_low = 0.2
gll_inner = np.array(
    [
        -0.8717401485096066,
        -0.5917001814331423,
        -0.20929921790247888,
        0.20929921790247888,
        0.5917001814331423,
        0.8717401485096066,
    ]
)


def padded_2(cells, sides, width):
    for axis, dim in sides:
        count = lax.axis_size(axis)
        ends = count - 1
        head = lax.slice_in_dim(cells, 0, width, axis=dim)
        tail = lax.slice_in_dim(cells, cells.shape[dim] - width, cells.shape[dim], axis=dim)
        from_prev = lax.ppermute(jnp.squeeze(tail, dim), axis, [(i, i + 1) for i in range(ends)])
        from_next = lax.ppermute(jnp.squeeze(head, dim), axis, [(i + 1, i) for i in range(ends)])
        cells = jnp.concatenate(
            [jnp.expand_dims(from_prev, dim), cells, jnp.expand_dims(from_next, dim)],
            axis=dim,
        )
    return cells


def group_partner(index, size, pairing):
    group = index // size
    return index + (pairing(group) - group) * size


def butterfly_sum(value, axes):
    for axis in axes:
        count = lax.axis_size(axis)
        size = count // 4
        stride = 1
        while stride < size:
            value = value + lax.ppermute(value, axis, [(i, i ^ stride) for i in range(count)])
            stride *= 2
        for pairing in (lambda g: 3 - g, lambda g: g ^ 1):
            pairs = [(i, group_partner(i, size, pairing)) for i in range(count)]
            value = value + lax.ppermute(value, axis, pairs)
    return value


def legendre_value(nodes, degree):
    previous = nodes * 0.0 + 1.0
    current = nodes
    for step in range(1, degree):
        following = ((2.0 * step + 1.0) * nodes * current - step * previous) / (step + 1.0)
        previous = current
        current = following
    return current


def gll_tables(poly_order):
    point_count = poly_order + 1
    gll_nodes = np.concatenate([np.array([-1.0]), gll_inner, np.array([1.0])])
    at_nodes = legendre_value(gll_nodes, poly_order)
    weights = 2.0 / (poly_order * point_count * at_nodes**2)
    differences = gll_nodes[:, None] - gll_nodes[None, :] + np.eye(point_count)
    derivative = at_nodes[:, None] / (at_nodes[None, :] * differences) * (1.0 - np.eye(point_count))
    end_value = poly_order * point_count / 4.0
    end_row = np.concatenate(
        [np.array([-end_value]), np.zeros(poly_order - 1), np.array([end_value])]
    )
    derivative = derivative + np.eye(point_count) * end_row[None, :]
    return (derivative, weights)


def forward_parts(field, mats):
    mat_x, mat_y, mat_z = mats
    size_x, size_y, size_z = field.shape
    grad_x = jnp.einsum("ia,ajk->ijk", mat_x, field, precision=local_precision)
    grad_y = jnp.einsum("ja,iak->ijk", mat_y, field, precision=local_precision)
    blocks = field.reshape(size_x, size_y, size_z // 128, 128)
    grad_z = jnp.einsum("ca,ijsa->ijsc", mat_z, blocks, precision=local_precision).reshape(field.shape)
    return (grad_x, grad_y, grad_z)


def backward_sum(parts, mats):
    mat_x, mat_y, mat_z = mats
    part_x, part_y, part_z = parts
    size_x, size_y, size_z = part_x.shape
    total = jnp.einsum("ai,ajk->ijk", mat_x, part_x, precision=local_precision)
    total = total + jnp.einsum("aj,iak->ijk", mat_y, part_y, precision=local_precision)
    blocks = part_z.reshape(size_x, size_y, size_z // 128, 128)
    total = total + jnp.einsum("ac,ijsa->ijsc", mat_z, blocks, precision=local_precision).reshape(
        part_x.shape
    )
    return total


def combine(padded, axis_dim, length, points):
    own = lax.slice_in_dim(padded, 1, length + 1, axis=axis_dim)
    left = lax.slice_in_dim(padded, 0, length, axis=axis_dim)
    right = lax.slice_in_dim(padded, 2, length + 2, axis=axis_dim)
    shape_list = [1, 1, 1]
    shape_list[axis_dim] = length
    position = (jnp.arange(length, dtype=jnp.int32) % points).reshape(shape_list)
    low_mask = (position == 0).astype(jnp.float32)
    high_mask = (position == points - 1).astype(jnp.float32)
    return own + low_mask * left + high_mask * right


def ghost_z(arrays, width):
    count = lax.axis_size("gz")
    head = jnp.stack([cells[..., :width] for cells in arrays])
    tail = jnp.stack([cells[..., cells.shape[-1] - width :] for cells in arrays])
    from_prev = lax.ppermute(tail, "gz", [(i, i + 1) for i in range(count - 1)])
    from_next = lax.ppermute(head, "gz", [(i + 1, i) for i in range(count - 1)])
    return [
        jnp.concatenate([from_prev[k], cells, from_next[k]], axis=-1)
        for k, cells in enumerate(arrays)
    ]


def assemble(field, points):
    size_x, size_y, size_z = field.shape
    padded = jnp.pad(field, ((0, 0), (0, 0), (1, 1)))
    padded = padded_2(padded, (("gx", 0), ("gy", 1)), 1)
    summed = combine(padded, 0, size_x, points)
    summed = combine(summed, 1, size_y, points)
    summed = combine(summed, 2, size_z, points)
    return summed


def per_device(right_side, coefficient, agg_weight, coarse_factor):
    points = ORDER + 1
    derivative, weights = gll_tables(ORDER)
    size_x, size_y, own_z = right_side.shape
    ghost = 64
    right_ext, coefficient = ghost_z([right_side, coefficient], ghost)
    size_z = own_z + 2 * ghost
    first = lax.axis_index("gz") * own_z - ghost
    global_z = first + jnp.arange(size_z, dtype=jnp.int32)
    inside = ((global_z >= 0) & (global_z < own_z * lax.axis_size("gz")))[None, None, :]
    mat_x = jnp.asarray(np.kron(np.eye(size_x // points), derivative), dtype=jnp.float32)
    mat_y = jnp.asarray(np.kron(np.eye(size_y // points), derivative), dtype=jnp.float32)
    mat_z = jnp.asarray(np.kron(np.eye(128 // points), derivative), dtype=jnp.float32)
    mats = (mat_x, mat_y, mat_z)
    squares = (mat_x * mat_x, mat_y * mat_y, mat_z * mat_z)
    weight_x = jnp.asarray(np.tile(weights, size_x // points), dtype=jnp.float32)
    weight_y = jnp.asarray(np.tile(weights, size_y // points), dtype=jnp.float32)
    weight_z = jnp.asarray(np.tile(weights, size_z // points), dtype=jnp.float32)
    scaled = (
        coefficient * weight_x[:, None, None] * weight_y[None, :, None] * weight_z[None, None, :]
    )
    diagonal = assemble(backward_sum((scaled, scaled, scaled), squares), points)
    inverse = jnp.where(inside, 1.0 / diagonal, 0.0)
    theta = (eig_high + eig_low) / 2.0
    delta = (eig_high - eig_low) / 2.0
    sigma = theta / delta
    residual = right_ext
    direction = inverse * residual / theta
    smoothed = direction
    rho = 1.0 / sigma
    for sweep in range(CHEB):
        grads = forward_parts(direction, mats)
        local = backward_sum((scaled * grads[0], scaled * grads[1], scaled * grads[2]), mats)
        residual = residual - assemble(local, points)
        if sweep + 1 < CHEB:
            rho_new = 1.0 / (2.0 * sigma - rho)
            direction = rho_new * rho * direction + 2.0 * rho_new / delta * inverse * residual
            smoothed = smoothed + direction
            rho = rho_new
    residual = residual[:, :, ghost : ghost + own_z]
    smoothed = smoothed[:, :, ghost : ghost + own_z]
    size_z = own_z
    aggregates = coarse_factor.shape[0]
    column_sums = jnp.sum(agg_weight * residual, axis=(0, 1))
    coarse_rhs = jnp.sum(column_sums.reshape(aggregates, size_z // aggregates), axis=1)
    partial_term = jnp.dot(coarse_rhs, coarse_factor, precision=highest)
    projected = butterfly_sum(partial_term, ("gy", "gz", "gx"))
    coarse_solution = jnp.dot(coarse_factor, projected, precision=highest)
    spread = jnp.repeat(coarse_solution, size_z // aggregates)
    pressure_update = smoothed + agg_weight * spread[None, None, :]
    return (pressure_update, coarse_solution)


def solution(mesh):
    return jax.shard_map(
        per_device,
        mesh=mesh,
        in_specs=(
            P("gx", "gy", "gz"),
            P("gx", "gy", "gz"),
            P("gx", "gy", "gz"),
            P(("gx", "gy", "gz"), None),
        ),
        out_specs=(P("gx", "gy", "gz"), P(("gx", "gy", "gz"))),
        check_vma=False,
    )
```
